512 devices in a mesh: row: 64 (over z, x), rep: 8 (over y, core).
Axes of the slice: x: 4, y: 4, z: 16, core: 2. Of those that a mesh axis runs over, the one named last changes fastest.
Arguments:
- features: bfloat16 [16384, 128], P('row', 'rep'), may hold values from -6 to 6
- owner_index: int32 [16384], P('row'), may hold values from 0 to 16383, as said below
- block_cols: int32 [128, 64], P('row', 'rep'), may hold values from 0 to 127, as said below
- block_count: int32 [128], P('row'), may hold values from 1 to 64, as said below
- tiles: bfloat16 [128, 64, 128, 128], P('row', 'rep'), may hold values from -0.109375 to 0.109375
- weight: bfloat16 [128, 256], P(None, 'rep'), may hold values from -0.75 to 0.75
- bias: float32 [256], P('rep'), may hold values from -4 to 4
- grad_out: bfloat16 [16384, 256], P('row', 'rep'), may hold values from -6 to 6
Outputs:
- hidden: bfloat16 [16384, 256], P('row', 'rep')
- weight_grad: float32 [128, 256], P(None, 'rep')
- bias_grad: float32 [256], P('rep')
The draws below stay inside these ranges and needn't reach their ends.
Inputs may be any that keep to these rules, and one draw needn't show every extreme that they name: `owner_index`: A permutation; the 256 rows of each loader shard hold exactly 4 positions of every partition's 2*128 rows. `block_cols`: the block columns of one block row are distinct. Block column c belongs to partition c // 2. Over all slots of one partition's 2 block rows, exactly 1 distinct block columns of each partition are named. `block_count`: some block row has all 64 slots live.
All inputs are finite; a program needn't handle non-finite values.
Results may differ from the reference program's by a relative error of at most 0.017.
Values may be sent and summed in bfloat16 or wider, within the bound.
No kernel may reach another device: no remote copies, remote signals or barrier semaphores. Data moves between devices by JAX's collectives and lax.ppermute only.
A program may use at most 64 MiB of HBM per device.

```python
import jax
import jax.numpy as jnp
from jax import lax

F_IN = 128
F_OUT = 256
BLK = 128
RB = 2
K = 64
NB = 128
NODES = 16384
PAIR = 4
USED = 1


def draw_owner_index(key, part):
    part_rows = RB * BLK
    owners = NODES // part_rows
    keys_first = jax.random.split(jax.random.fold_in(key, 11), owners)
    slot_perm = jax.vmap(lambda k: jax.random.permutation(k, part_rows))(keys_first)
    values = slot_perm + (jnp.arange(owners, dtype=jnp.int32) * part_rows)[:, None]
    values = values.reshape(owners, owners, PAIR).transpose(1, 0, 2).reshape(owners, part_rows)
    keys_second = jax.random.split(jax.random.fold_in(key, 12), owners)
    shuffled = jax.vmap(lambda k, v: jax.random.permutation(k, v))(keys_second, values)
    return shuffled.reshape(NODES).astype(jnp.int32)


def draw_block_cols(key, part):
    owners = NB // RB
    allowed_count = owners * USED
    keys_local = jax.random.split(jax.random.fold_in(key, 21), owners * owners)
    local = jax.vmap(lambda k: jax.random.permutation(k, RB)[:USED])(keys_local)
    local = local.reshape(owners, owners, USED) + (jnp.arange(owners, dtype=jnp.int32) * RB)[None, :, None]
    allowed = local.reshape(owners, allowed_count)
    keys_order = jax.random.split(jax.random.fold_in(key, 22), owners)
    shuffled = jax.vmap(lambda k, v: jax.random.permutation(k, v))(keys_order, allowed)
    picks = (jnp.arange(RB, dtype=jnp.int32)[:, None] * K + jnp.arange(K, dtype=jnp.int32)[None, :]) % allowed_count
    rows = shuffled[:, picks].reshape(NB, K)
    keys_rows = jax.random.split(jax.random.fold_in(key, 23), NB)
    rows = jax.vmap(lambda k, v: jax.random.permutation(k, v))(keys_rows, rows)
    return rows.astype(jnp.int32)


def draw_block_count(key, part):
    first = jax.random.randint(jax.random.fold_in(key, 31), (NB,), 1, K + 1)
    second = jax.random.randint(jax.random.fold_in(key, 32), (NB,), 1, K + 1)
    counts = jnp.minimum(first, second)
    where_full = jax.random.randint(jax.random.fold_in(key, 33), (), 0, NB)
    counts = counts.at[where_full].set(K)
    return counts.astype(jnp.int32)


def block_scale(stream_key, shape, cuts, low, largest):
    level, own = 1.0, jax.random.fold_in(stream_key, 6)
    for axis_at, shards_of in cuts:
        steps = jnp.exp(jax.random.uniform(jax.random.fold_in(own, axis_at), (shards_of,), jnp.float32, low / len(cuts), largest / len(cuts)))
        level = level * jnp.repeat(steps, shape[axis_at] // shards_of).reshape([-1 if axis == axis_at else 1 for axis in range(len(shape))])
    return level


def scatter_about(own_key, extent, deviation, most, pieces=(), held_as=jnp.bfloat16):
    array = deviation * jax.random.normal(own_key, extent, jnp.float32)
    if pieces:
        array = array * block_scale(own_key, extent, pieces, -0.22, 0.18)
    return jnp.clip(array, -most, most).astype(held_as)


def setup_inputs(seed: int = 0) -> dict:
    streams_of = jax.random.split(jax.random.key(seed), 9)
    features = scatter_about(streams_of[0], (NODES, F_IN), 1.0, 6.0, ((0, 64), (1, 8)))
    owner_index = draw_owner_index(jax.random.fold_in(streams_of[8], 71), 0)
    block_cols = draw_block_cols(jax.random.fold_in(streams_of[8], 71), 0)
    block_count = draw_block_count(jax.random.fold_in(streams_of[8], 71), 0)
    tiles = scatter_about(streams_of[4], (NB, K, BLK, BLK), (K * BLK // 3) ** -0.5, 0.109375, ((0, 64), (1, 8)))
    weight = scatter_about(streams_of[5], (F_IN, F_OUT), (F_IN // 2) ** -0.5, 0.75, ((1, 8),))
    bias = scatter_about(streams_of[6], (F_OUT,), 0.7, 4.0, ((0, 8),), jnp.float32)
    grad_out = scatter_about(streams_of[7], (NODES, F_OUT), 1.0, 6.0, ((0, 64), (1, 8)))
    return {"features": features, "owner_index": owner_index, "block_cols": block_cols, "block_count": block_count, "tiles": tiles, "weight": weight, "bias": bias, "grad_out": grad_out}


def reference(features, owner_index, block_cols, block_count, tiles, weight, bias, grad_out):
    owned = jnp.zeros_like(features).at[owner_index].set(features)
    blocks = block_cols.shape[0]
    size_blk = tiles.shape[2]
    table = owned.reshape(blocks, size_blk, features.shape[1])
    slot_ids = jnp.arange(block_cols.shape[1], dtype=jnp.int32)

    def one_row(packed):
        tile_row, cols_row, count_row = packed
        picked = table[cols_row].astype(jnp.float32)
        live = (slot_ids < count_row)[:, None, None]
        picked = jnp.where(live, picked, jnp.float32(0.0))
        return jnp.einsum("kij,kjc->ic", tile_row.astype(jnp.float32), picked)

    agg = lax.map(one_row, (tiles, block_cols, block_count))
    agg = agg.reshape(features.shape[0], features.shape[1]).astype(jnp.bfloat16)
    pre = jnp.dot(agg, weight, preferred_element_type=jnp.float32) + bias
    hidden = jax.nn.silu(pre).astype(jnp.bfloat16)
    sig = jax.nn.sigmoid(pre)
    dpre = (grad_out.astype(jnp.float32) * sig * (1.0 + pre * (1.0 - sig))).astype(jnp.bfloat16)
    weight_grad = jnp.dot(agg.T, dpre, preferred_element_type=jnp.float32)
    bias_grad = jnp.sum(dpre.astype(jnp.float32), axis=0)
    return hidden, weight_grad, bias_grad
```

```python
import jax
import jax.numpy as jnp
from jax import lax
from jax.sharding import PartitionSpec as P


def sum_over(x, axis_name, count):
    rows = x.shape[0]
    pieces = x.reshape((count, rows // count) + x.shape[1:])
    got = lax.all_to_all(pieces, axis_name, 0, 0, tiled=True)
    reduced = jnp.sum(got.astype(jnp.float32), axis=0)
    return reduced


def spread(x, axis_name, count):
    wide = jnp.broadcast_to(x[None], (count,) + x.shape)
    return lax.all_to_all(wide, axis_name, 0, 0, tiled=True)


def on_device(features, owner_index, block_cols, block_count, tiles, weight, bias, grad_out):
    rows_part, cols_dev = features.shape
    parts = lax.axis_size("row")
    reps = lax.axis_size("rep")
    per_pair = rows_part // parts
    rb, slots_dev, size_blk = tiles.shape[0], tiles.shape[1], tiles.shape[2]

    destination = owner_index // rows_part
    order = jnp.argsort(destination, stable=True)
    send_rows = features[order]
    send_pos = (owner_index[order] % rows_part).astype(jnp.bfloat16)
    packet = jnp.concatenate([send_rows.T, send_pos[None, :]], axis=0)
    everyone = spread(packet, "row", parts)
    width = cols_dev + 1
    grouped = everyone.reshape(parts, width, parts, per_pair).transpose(2, 1, 0, 3).reshape(parts, width, rows_part)
    pos = grouped[:, cols_dev, :].astype(jnp.int32)
    values = grouped[:, :cols_dev, :]

    cols_all = lax.all_gather(block_cols, "rep", axis=1, tiled=True)
    part_of = cols_all // rb
    half_of = cols_all % rb
    part_ids = jnp.arange(parts, dtype=jnp.int32)
    hit = part_of[None, :, :] == part_ids[:, None, None]
    half = jnp.max(jnp.where(hit, half_of[None, :, :], 0), axis=(1, 2))
    node_ids = jnp.arange(size_blk, dtype=jnp.int32)
    target = half[:, None, None] * size_blk + node_ids[None, None, :]
    pick = (pos[:, :, None] == target).astype(jnp.bfloat16)
    needed = jnp.einsum("qfg,qgn->qfn", values, pick, preferred_element_type=jnp.float32).astype(jnp.bfloat16)

    peer_parts = part_of.reshape(rb, reps, slots_dev).transpose(1, 0, 2)
    outgoing = needed[peer_parts]
    incoming = lax.all_to_all(outgoing, "rep", 0, 0, tiled=True)

    slot_ids = lax.axis_index("rep") * slots_dev + jnp.arange(slots_dev, dtype=jnp.int32)
    live = slot_ids[None, :] < block_count[:, None]
    tiles_live = jnp.where(live[:, :, None, None], tiles, jnp.zeros_like(tiles))
    partial = jnp.einsum("rsin,jrsfn->rijf", tiles_live, incoming, preferred_element_type=jnp.float32)
    partial = partial.reshape(rows_part, reps * cols_dev)

    agg_part = sum_over(partial, "rep", reps).astype(jnp.bfloat16)
    agg = spread(agg_part, "rep", reps).reshape(rows_part, reps * cols_dev)

    pre = jnp.dot(agg, weight, preferred_element_type=jnp.float32) + bias
    hidden = jax.nn.silu(pre).astype(jnp.bfloat16)
    sig = jax.nn.sigmoid(pre)
    dpre = (grad_out.astype(jnp.float32) * sig * (1.0 + pre * (1.0 - sig))).astype(jnp.bfloat16)
    weight_term = jnp.dot(agg.T, dpre, preferred_element_type=jnp.float32)
    bias_term = jnp.sum(dpre.astype(jnp.float32), axis=0)

    flat = jnp.concatenate([weight_term.reshape(-1), bias_term])
    lanes = 128
    chunk = lanes * (-(-flat.shape[0] // (parts * lanes)))
    flat = jnp.pad(flat, (0, parts * chunk - flat.shape[0])).reshape(parts, chunk)
    total = spread(sum_over(flat, "row", parts), "row", parts).reshape(-1)
    n_w = weight_term.size
    weight_grad = total[:n_w].reshape(weight_term.shape)
    bias_grad = total[n_w:n_w + bias_term.shape[0]]
    return (hidden, weight_grad, bias_grad)


def solution(mesh):
    placed = (
        P("row", "rep"),
        P("row"),
        P("row", "rep"),
        P("row"),
        P("row", "rep", None, None),
        P(None, "rep"),
        P("rep"),
        P("row", "rep"),
    )
    return jax.shard_map(
        on_device,
        mesh=mesh,
        in_specs=placed,
        out_specs=(P("row", "rep"), P(None, "rep"), P("rep")),
        check_vma=False,
    )
```

```python
import jax
import jax.numpy as jnp
from jax import lax
from jax.sharding import PartitionSpec as P


def sum_over(x, axis_name, count):
    rows = x.shape[0]
    pieces = x.reshape((count, rows // count) + x.shape[1:])
    got = lax.all_to_all(pieces, axis_name, 0, 0, tiled=True)
    reduced = jnp.sum(got.astype(jnp.float32), axis=0)
    return reduced


def spread(x, axis_name, count):
    wide = jnp.broadcast_to(x[None], (count,) + x.shape)
    return lax.all_to_all(wide, axis_name, 0, 0, tiled=True)


def on_device(features, owner_index, block_cols, block_count, tiles, weight, bias, grad_out):
    rows_part, cols_dev = features.shape
    parts = lax.axis_size("row")
    reps = lax.axis_size("rep")
    per_pair = rows_part // parts
    rb, slots_dev, size_blk = tiles.shape[0], tiles.shape[1], tiles.shape[2]

    destination = owner_index // rows_part
    same = destination[:, None] == destination[None, :]
    before = jnp.arange(rows_part)[:, None] > jnp.arange(rows_part)[None, :]
    rank = jnp.sum(same & before, axis=1)
    slot = destination * per_pair + rank
    place = (slot[:, None] == jnp.arange(rows_part)[None, :]).astype(jnp.bfloat16)
    pos_row = (owner_index % rows_part).astype(jnp.bfloat16)
    loader = jnp.concatenate([features.T, pos_row[None, :]], axis=0)
    packet = jnp.dot(loader, place, preferred_element_type=jnp.float32).astype(jnp.bfloat16)
    width = cols_dev + 1
    packet = packet.reshape(width, parts, per_pair)
    wide = jnp.broadcast_to(packet[None], (parts,) + packet.shape)
    grouped = lax.all_to_all(wide, "row", 0, 3, tiled=True).reshape(width, parts, rows_part)
    pos = grouped[cols_dev].astype(jnp.int32)
    values = grouped[:cols_dev]

    cols_all = lax.all_gather(block_cols, "rep", axis=1, tiled=True)
    part_of = cols_all // rb
    half_of = cols_all % rb
    part_ids = jnp.arange(parts, dtype=jnp.int32)
    hit = part_of[None, :, :] == part_ids[:, None, None]
    half = jnp.max(jnp.where(hit, half_of[None, :, :], 0), axis=(1, 2))
    node_ids = jnp.arange(size_blk, dtype=jnp.int32)
    target = half[:, None, None] * size_blk + node_ids[None, None, :]
    pick = (pos[:, :, None] == target).astype(jnp.bfloat16)
    needed = jnp.einsum("fqg,qgn->qfn", values, pick, preferred_element_type=jnp.float32).astype(jnp.bfloat16)

    peer_parts = part_of.reshape(rb, reps, slots_dev).transpose(1, 0, 2)
    outgoing = needed[peer_parts]
    incoming = lax.all_to_all(outgoing, "rep", 0, 0, tiled=True)

    slot_ids = lax.axis_index("rep") * slots_dev + jnp.arange(slots_dev, dtype=jnp.int32)
    live = slot_ids[None, :] < block_count[:, None]
    tiles_live = jnp.where(live[:, :, None, None], tiles, jnp.zeros_like(tiles))
    partial = jnp.einsum("rsin,jrsfn->rijf", tiles_live, incoming, preferred_element_type=jnp.float32)
    partial = partial.reshape(rows_part, reps * cols_dev)

    shares = spread(partial.astype(jnp.bfloat16), "rep", reps)
    agg = jnp.sum(shares.astype(jnp.float32), axis=0).astype(jnp.bfloat16)

    pre = jnp.dot(agg, weight, preferred_element_type=jnp.float32) + bias
    hidden = jax.nn.silu(pre).astype(jnp.bfloat16)
    sig = jax.nn.sigmoid(pre)
    dpre = (grad_out.astype(jnp.float32) * sig * (1.0 + pre * (1.0 - sig))).astype(jnp.bfloat16)
    weight_term = jnp.dot(agg.T, dpre, preferred_element_type=jnp.float32)
    bias_term = jnp.sum(dpre.astype(jnp.float32), axis=0)

    flat = jnp.concatenate([weight_term.reshape(-1), bias_term])
    lanes = 128
    chunk = lanes * (-(-flat.shape[0] // (parts * lanes)))
    flat = jnp.pad(flat, (0, parts * chunk - flat.shape[0])).reshape(parts, chunk)
    total = spread(sum_over(flat, "row", parts), "row", parts).reshape(-1)
    n_w = weight_term.size
    weight_grad = total[:n_w].reshape(weight_term.shape)
    bias_grad = total[n_w:n_w + bias_term.shape[0]]
    return (hidden, weight_grad, bias_grad)


def solution(mesh):
    placed = (
        P("row", "rep"),
        P("row"),
        P("row", "rep"),
        P("row"),
        P("row", "rep", None, None),
        P(None, "rep"),
        P("rep"),
        P("row", "rep"),
    )
    return jax.shard_map(
        on_device,
        mesh=mesh,
        in_specs=placed,
        out_specs=(P("row", "rep"), P(None, "rep"), P("rep")),
        check_vma=False,
    )
```

```python
import jax
import jax.numpy as jnp
from jax import lax
from jax.sharding import Mesh, PartitionSpec as P

ROW = ("hi", "lo")


def sum_over(x, axis_name, count):
    rows = x.shape[0]
    pieces = x.reshape((count, rows // count) + x.shape[1:])
    got = lax.all_to_all(pieces, axis_name, 0, 0, tiled=True)
    reduced = jnp.sum(got.astype(jnp.float32), axis=0)
    return reduced


def spread(x, axis_name, count):
    wide = jnp.broadcast_to(x[None], (count,) + x.shape)
    return lax.all_to_all(wide, axis_name, 0, 0, tiled=True)


def on_device(features, owner_index, block_cols, block_count, tiles, weight, bias, grad_out):
    rows_part, cols_dev = features.shape
    parts = lax.axis_size("hi") * lax.axis_size("lo")
    reps = lax.axis_size("rep")
    per_pair = rows_part // parts
    rb, slots_dev, size_blk = tiles.shape[0], tiles.shape[1], tiles.shape[2]

    destination = owner_index // rows_part
    same = destination[:, None] == destination[None, :]
    before = jnp.arange(rows_part)[:, None] > jnp.arange(rows_part)[None, :]
    rank = jnp.sum(same & before, axis=1)
    slot = destination * per_pair + rank
    place = (slot[:, None] == jnp.arange(rows_part)[None, :]).astype(jnp.bfloat16)
    pos_row = (owner_index % rows_part).astype(jnp.bfloat16)
    loader = jnp.concatenate([features.T, pos_row[None, :]], axis=0)
    packet = jnp.dot(loader, place, preferred_element_type=jnp.float32).astype(jnp.bfloat16)
    width = cols_dev + 1
    packet = packet.reshape(width, parts, per_pair)
    for level in ("lo", "hi"):
        wide = jnp.broadcast_to(packet[None], (lax.axis_size(level),) + packet.shape)
        packet = lax.all_to_all(wide, level, 0, 3, tiled=True)[0]
    grouped = packet
    pos = grouped[cols_dev].astype(jnp.int32)
    values = grouped[:cols_dev]

    cols_all = lax.all_gather(block_cols, "rep", axis=1, tiled=True)
    part_of = cols_all // rb
    half_of = cols_all % rb
    part_ids = jnp.arange(parts, dtype=jnp.int32)
    hit = part_of[None, :, :] == part_ids[:, None, None]
    half = jnp.max(jnp.where(hit, half_of[None, :, :], 0), axis=(1, 2))
    node_ids = jnp.arange(size_blk, dtype=jnp.int32)
    target = half[:, None, None] * size_blk + node_ids[None, None, :]
    pick = (pos[:, :, None] == target).astype(jnp.bfloat16)
    needed = jnp.einsum("fqg,qgn->qfn", values, pick, preferred_element_type=jnp.float32).astype(jnp.bfloat16)

    peer_parts = part_of.reshape(rb, reps, slots_dev).transpose(1, 0, 2)
    outgoing = needed[peer_parts]
    incoming = lax.all_to_all(outgoing, "rep", 0, 0, tiled=True)

    slot_ids = lax.axis_index("rep") * slots_dev + jnp.arange(slots_dev, dtype=jnp.int32)
    live = slot_ids[None, :] < block_count[:, None]
    tiles_live = jnp.where(live[:, :, None, None], tiles, jnp.zeros_like(tiles))
    partial = jnp.einsum("rsin,jrsfn->rijf", tiles_live, incoming, preferred_element_type=jnp.float32)
    partial = partial.reshape(rows_part, reps * cols_dev)

    shares = spread(partial.astype(jnp.bfloat16), "rep", reps)
    agg = jnp.sum(shares.astype(jnp.float32), axis=0).astype(jnp.bfloat16)

    pre = jnp.dot(agg, weight, preferred_element_type=jnp.float32) + bias
    hidden = jax.nn.silu(pre).astype(jnp.bfloat16)
    sig = jax.nn.sigmoid(pre)
    dpre = (grad_out.astype(jnp.float32) * sig * (1.0 + pre * (1.0 - sig))).astype(jnp.bfloat16)
    weight_term = jnp.dot(agg.T, dpre, preferred_element_type=jnp.float32)
    bias_term = jnp.sum(dpre.astype(jnp.float32), axis=0)

    flat = jnp.concatenate([weight_term.reshape(-1), bias_term])
    lanes = 128
    chunk = lanes * (-(-flat.shape[0] // (parts * lanes)))
    flat = jnp.pad(flat, (0, parts * chunk - flat.shape[0])).reshape(parts, chunk)
    total = spread(sum_over(flat, ROW, parts), ROW, parts).reshape(-1)
    n_w = weight_term.size
    weight_grad = total[:n_w].reshape(weight_term.shape)
    bias_grad = total[n_w:n_w + bias_term.shape[0]]
    return (hidden, weight_grad, bias_grad)


def solution(mesh):
    row_size, rep_size = mesh.shape["row"], mesh.shape["rep"]
    lo_size = 4 if row_size % 4 == 0 else 1
    split = Mesh(mesh.devices.reshape(row_size // lo_size, lo_size, rep_size), ("hi", "lo", "rep"))
    placed = (
        P(ROW, "rep"),
        P(ROW),
        P(ROW, "rep"),
        P(ROW),
        P(ROW, "rep", None, None),
        P(None, "rep"),
        P("rep"),
        P(ROW, "rep"),
    )
    return jax.shard_map(
        on_device,
        mesh=split,
        in_specs=placed,
        out_specs=(P(ROW, "rep"), P(None, "rep"), P("rep")),
        check_vma=False,
    )
```

```python
import jax
import jax.numpy as jnp
from jax import lax
from jax.sharding import PartitionSpec as P


def sum_over(x, axis_name, count):
    rows = x.shape[0]
    pieces = x.reshape((count, rows // count) + x.shape[1:])
    got = lax.all_to_all(pieces, axis_name, 0, 0, tiled=True)
    reduced = jnp.sum(got.astype(jnp.float32), axis=0)
    return reduced


def spread(x, axis_name, count):
    wide = jnp.broadcast_to(x[None], (count,) + x.shape)
    return lax.all_to_all(wide, axis_name, 0, 0, tiled=True)


def on_device(features, owner_index, block_cols, block_count, tiles, weight, bias, grad_out):
    rows_part, cols_dev = features.shape
    parts = lax.axis_size("row")
    reps = lax.axis_size("rep")
    per_pair = rows_part // parts
    rb, slots_dev, size_blk = tiles.shape[0], tiles.shape[1], tiles.shape[2]

    destination = owner_index // rows_part
    same = destination[:, None] == destination[None, :]
    before = jnp.arange(rows_part)[:, None] > jnp.arange(rows_part)[None, :]
    rank = jnp.sum(same & before, axis=1)
    slot = destination * per_pair + rank
    place = (slot[:, None] == jnp.arange(rows_part)[None, :]).astype(jnp.bfloat16)
    pos_row = (owner_index % rows_part).astype(jnp.bfloat16)
    loader = jnp.concatenate([features.T, pos_row[None, :]], axis=0)
    packet = jnp.dot(loader, place, preferred_element_type=jnp.float32).astype(jnp.bfloat16)
    width = cols_dev + 1
    packet = packet.reshape(width, parts, per_pair)
    wide = jnp.broadcast_to(packet[None], (parts,) + packet.shape)
    grouped = lax.all_to_all(wide, "row", 0, 3, tiled=True).reshape(width, parts, rows_part)
    pos = grouped[cols_dev].astype(jnp.int32)
    values = grouped[:cols_dev]

    cols_all = lax.all_gather(block_cols, "rep", axis=1, tiled=True)
    part_of = cols_all // rb
    half_of = cols_all % rb
    part_ids = jnp.arange(parts, dtype=jnp.int32)
    hit = part_of[None, :, :] == part_ids[:, None, None]
    half = jnp.max(jnp.where(hit, half_of[None, :, :], 0), axis=(1, 2))
    node_ids = jnp.arange(size_blk, dtype=jnp.int32)
    target = half[:, None, None] * size_blk + node_ids[None, None, :]
    pick = (pos[:, :, None] == target).astype(jnp.bfloat16)
    needed = jnp.einsum("fqg,qgn->qfn", values, pick, preferred_element_type=jnp.float32).astype(jnp.bfloat16)

    peer_parts = part_of.reshape(rb, reps, slots_dev).transpose(1, 0, 2).reshape(-1)
    choose = (peer_parts[:, None] == part_ids[None, :]).astype(jnp.bfloat16)
    outgoing = jnp.dot(choose, needed.reshape(parts, -1), preferred_element_type=jnp.float32)
    outgoing = outgoing.astype(jnp.bfloat16).reshape(reps, rb, slots_dev, cols_dev, size_blk)
    incoming = lax.all_to_all(outgoing, "rep", 0, 0, tiled=True)

    slot_ids = lax.axis_index("rep") * slots_dev + jnp.arange(slots_dev, dtype=jnp.int32)
    live = slot_ids[None, :] < block_count[:, None]
    tiles_live = jnp.where(live[:, :, None, None], tiles, jnp.zeros_like(tiles))
    partial = jnp.einsum("rsin,jrsfn->rijf", tiles_live, incoming, preferred_element_type=jnp.float32)
    partial = partial.reshape(rows_part, reps * cols_dev)

    shares = spread(partial.astype(jnp.bfloat16), "rep", reps)
    agg = jnp.sum(shares.astype(jnp.float32), axis=0).astype(jnp.bfloat16)

    pre = jnp.dot(agg, weight, preferred_element_type=jnp.float32) + bias
    hidden = jax.nn.silu(pre).astype(jnp.bfloat16)
    sig = jax.nn.sigmoid(pre)
    dpre = (grad_out.astype(jnp.float32) * sig * (1.0 + pre * (1.0 - sig))).astype(jnp.bfloat16)
    weight_term = jnp.dot(agg.T, dpre, preferred_element_type=jnp.float32)
    bias_term = jnp.sum(dpre.astype(jnp.float32), axis=0)

    flat = jnp.concatenate([weight_term.reshape(-1), bias_term])
    lanes = 128
    chunk = lanes * (-(-flat.shape[0] // (parts * lanes)))
    flat = jnp.pad(flat, (0, parts * chunk - flat.shape[0])).reshape(parts, chunk)
    total = spread(sum_over(flat, "row", parts), "row", parts).reshape(-1)
    n_w = weight_term.size
    weight_grad = total[:n_w].reshape(weight_term.shape)
    bias_grad = total[n_w:n_w + bias_term.shape[0]]
    return (hidden, weight_grad, bias_grad)


def solution(mesh):
    placed = (
        P("row", "rep"),
        P("row"),
        P("row", "rep"),
        P("row"),
        P("row", "rep", None, None),
        P(None, "rep"),
        P("rep"),
        P("row", "rep"),
    )
    return jax.shard_map(
        on_device,
        mesh=mesh,
        in_specs=placed,
        out_specs=(P("row", "rep"), P(None, "rep"), P("rep")),
        check_vma=False,
    )
```

```python
import jax
import jax.numpy as jnp
from jax import lax
from jax.sharding import PartitionSpec as P


def sum_over(x, axis_name, count):
    rows = x.shape[0]
    pieces = x.reshape((count, rows // count) + x.shape[1:])
    got = lax.all_to_all(pieces, axis_name, 0, 0, tiled=True)
    reduced = jnp.sum(got.astype(jnp.float32), axis=0)
    return reduced


def spread(x, axis_name, count):
    wide = jnp.broadcast_to(x[None], (count,) + x.shape)
    return lax.all_to_all(wide, axis_name, 0, 0, tiled=True)


def on_device(features, owner_index, block_cols, block_count, tiles, weight, bias, grad_out):
    rows_part, cols_dev = features.shape
    parts = lax.axis_size("row")
    reps = lax.axis_size("rep")
    per_pair = rows_part // parts
    rb, slots_dev, size_blk = tiles.shape[0], tiles.shape[1], tiles.shape[2]

    destination = owner_index // rows_part
    same = destination[:, None] == destination[None, :]
    before = jnp.arange(rows_part)[:, None] > jnp.arange(rows_part)[None, :]
    rank = jnp.sum(same & before, axis=1)
    slot = rank * parts + destination
    place = (slot[:, None] == jnp.arange(rows_part)[None, :]).astype(jnp.bfloat16)
    pos_row = (owner_index % rows_part).astype(jnp.bfloat16)
    loader = jnp.concatenate([features.T, pos_row[None, :]], axis=0)
    packet = jnp.dot(loader, place, preferred_element_type=jnp.float32).astype(jnp.bfloat16)
    width = cols_dev + 1
    packet = packet.reshape(width, per_pair, parts)
    wide = jnp.broadcast_to(packet[None], (parts,) + packet.shape)
    grouped = lax.all_to_all(wide, "row", 0, 2, tiled=True)[0]
    pos = grouped[cols_dev].T.astype(jnp.int32)
    values = grouped[:cols_dev]

    cols_all = lax.all_gather(block_cols, "rep", axis=1, tiled=True)
    part_of = cols_all // rb
    half_of = cols_all % rb
    part_ids = jnp.arange(parts, dtype=jnp.int32)
    hit = part_of[None, :, :] == part_ids[:, None, None]
    half = jnp.max(jnp.where(hit, half_of[None, :, :], 0), axis=(1, 2))
    node_ids = jnp.arange(size_blk, dtype=jnp.int32)
    target = half[:, None, None] * size_blk + node_ids[None, None, :]
    pick = (pos[:, :, None] == target).astype(jnp.bfloat16)
    needed = jnp.einsum("fgq,qgn->qfn", values, pick, preferred_element_type=jnp.float32).astype(jnp.bfloat16)

    peer_parts = part_of.reshape(rb, reps, slots_dev).transpose(1, 0, 2).reshape(-1)
    choose = (peer_parts[:, None] == part_ids[None, :]).astype(jnp.bfloat16)
    outgoing = jnp.dot(choose, needed.reshape(parts, -1), preferred_element_type=jnp.float32)
    outgoing = outgoing.astype(jnp.bfloat16).reshape(reps, rb, slots_dev, cols_dev, size_blk)
    incoming = lax.all_to_all(outgoing, "rep", 0, 0, tiled=True)

    slot_ids = lax.axis_index("rep") * slots_dev + jnp.arange(slots_dev, dtype=jnp.int32)
    live = slot_ids[None, :] < block_count[:, None]
    tiles_live = jnp.where(live[:, :, None, None], tiles, jnp.zeros_like(tiles))
    partial = jnp.einsum("rsin,jrsfn->rijf", tiles_live, incoming, preferred_element_type=jnp.float32)
    partial = partial.reshape(rows_part, reps * cols_dev)

    shares = spread(partial.astype(jnp.bfloat16), "rep", reps)
    agg = jnp.sum(shares.astype(jnp.float32), axis=0).astype(jnp.bfloat16)

    pre = jnp.dot(agg, weight, preferred_element_type=jnp.float32) + bias
    hidden = jax.nn.silu(pre).astype(jnp.bfloat16)
    sig = jax.nn.sigmoid(pre)
    dpre = (grad_out.astype(jnp.float32) * sig * (1.0 + pre * (1.0 - sig))).astype(jnp.bfloat16)
    weight_term = jnp.dot(agg.T, dpre, preferred_element_type=jnp.float32)
    bias_term = jnp.sum(dpre.astype(jnp.float32), axis=0)

    flat = jnp.concatenate([weight_term.reshape(-1), bias_term])
    lanes = 128
    chunk = lanes * (-(-flat.shape[0] // (parts * lanes)))
    flat = jnp.pad(flat, (0, parts * chunk - flat.shape[0])).reshape(parts, chunk)
    total = spread(sum_over(flat, "row", parts), "row", parts).reshape(-1)
    n_w = weight_term.size
    weight_grad = total[:n_w].reshape(weight_term.shape)
    bias_grad = total[n_w:n_w + bias_term.shape[0]]
    return (hidden, weight_grad, bias_grad)


def solution(mesh):
    placed = (
        P("row", "rep"),
        P("row"),
        P("row", "rep"),
        P("row"),
        P("row", "rep", None, None),
        P(None, "rep"),
        P("rep"),
        P("row", "rep"),
    )
    return jax.shard_map(
        on_device,
        mesh=mesh,
        in_specs=placed,
        out_specs=(P("row", "rep"), P(None, "rep"), P("rep")),
        check_vma=False,
    )
```

```python
import jax
import jax.numpy as jnp
from jax import lax
from jax.sharding import PartitionSpec as P


def sum_over(x, axis_name, count):
    rows = x.shape[0]
    pieces = x.reshape((count, rows // count) + x.shape[1:])
    got = lax.all_to_all(pieces, axis_name, 0, 0, tiled=True)
    reduced = jnp.sum(got.astype(jnp.float32), axis=0)
    return reduced


def spread(x, axis_name, count):
    wide = jnp.broadcast_to(x[None], (count,) + x.shape)
    return lax.all_to_all(wide, axis_name, 0, 0, tiled=True)


def on_device(features, owner_index, block_cols, block_count, tiles, weight, bias, grad_out):
    rows_part, cols_dev = features.shape
    parts = lax.axis_size("row")
    reps = lax.axis_size("rep")
    per_pair = rows_part // parts
    rb, slots_dev, size_blk = tiles.shape[0], tiles.shape[1], tiles.shape[2]

    destination = owner_index // rows_part
    same = destination[:, None] == destination[None, :]
    before = jnp.arange(rows_part)[:, None] > jnp.arange(rows_part)[None, :]
    rank = jnp.sum(same & before, axis=1)
    slot = rank * parts + destination
    place = (slot[:, None] == jnp.arange(rows_part)[None, :]).astype(jnp.bfloat16)
    pos_row = (owner_index % rows_part).astype(jnp.bfloat16)
    loader = jnp.concatenate([features.T, pos_row[None, :]], axis=0)
    packet = jnp.dot(loader, place, preferred_element_type=jnp.float32).astype(jnp.bfloat16)
    width = cols_dev + 1
    packet = packet.reshape(width, per_pair, parts)
    wide = jnp.broadcast_to(packet[None], (parts,) + packet.shape)
    grouped = lax.all_to_all(wide, "row", 0, 2, tiled=True)[0]
    pos = grouped[cols_dev].T.astype(jnp.int32)
    values = grouped[:cols_dev]

    cols_all = lax.all_gather(block_cols, "rep", axis=1, tiled=True)
    part_of = cols_all // rb
    half_of = cols_all % rb
    part_ids = jnp.arange(parts, dtype=jnp.int32)
    hit = part_of[None, :, :] == part_ids[:, None, None]
    half = jnp.max(jnp.where(hit, half_of[None, :, :], 0), axis=(1, 2))
    node_ids = jnp.arange(size_blk, dtype=jnp.int32)
    target = half[:, None, None] * size_blk + node_ids[None, None, :]
    pick = (pos[:, :, None] == target).astype(jnp.bfloat16)
    needed = jnp.einsum("fgq,qgn->qfn", grouped, pick, preferred_element_type=jnp.float32).astype(jnp.bfloat16)
    needed = needed[:, :cols_dev, :]

    peer_parts = part_of.reshape(rb, reps, slots_dev).transpose(1, 0, 2).reshape(-1)
    choose = (peer_parts[:, None] == part_ids[None, :]).astype(jnp.bfloat16)
    outgoing = jnp.dot(choose, needed.reshape(parts, -1), preferred_element_type=jnp.float32)
    outgoing = outgoing.astype(jnp.bfloat16).reshape(reps, rb, slots_dev, cols_dev, size_blk)
    incoming = lax.all_to_all(outgoing, "rep", 0, 0, tiled=True)

    slot_ids = lax.axis_index("rep") * slots_dev + jnp.arange(slots_dev, dtype=jnp.int32)
    live = slot_ids[None, :] < block_count[:, None]
    tiles_live = jnp.where(live[:, :, None, None], tiles, jnp.zeros_like(tiles))
    partial = jnp.einsum("rsin,jrsfn->rijf", tiles_live, incoming, preferred_element_type=jnp.float32)
    partial = partial.reshape(rows_part, reps * cols_dev)

    shares = spread(partial.astype(jnp.bfloat16), "rep", reps)
    agg = jnp.sum(shares.astype(jnp.float32), axis=0).astype(jnp.bfloat16)

    pre = jnp.dot(agg, weight, preferred_element_type=jnp.float32) + bias
    hidden = jax.nn.silu(pre).astype(jnp.bfloat16)
    sig = jax.nn.sigmoid(pre)
    dpre = (grad_out.astype(jnp.float32) * sig * (1.0 + pre * (1.0 - sig))).astype(jnp.bfloat16)
    weight_term = jnp.dot(agg.T, dpre, preferred_element_type=jnp.float32)
    bias_term = jnp.sum(dpre.astype(jnp.float32), axis=0)

    flat = jnp.concatenate([weight_term.reshape(-1), bias_term])
    lanes = 128
    chunk = lanes * (-(-flat.shape[0] // (parts * lanes)))
    flat = jnp.pad(flat, (0, parts * chunk - flat.shape[0])).reshape(parts, chunk)
    total = spread(sum_over(flat, "row", parts), "row", parts).reshape(-1)
    n_w = weight_term.size
    weight_grad = total[:n_w].reshape(weight_term.shape)
    bias_grad = total[n_w:n_w + bias_term.shape[0]]
    return (hidden, weight_grad, bias_grad)


def solution(mesh):
    placed = (
        P("row", "rep"),
        P("row"),
        P("row", "rep"),
        P("row"),
        P("row", "rep", None, None),
        P(None, "rep"),
        P("rep"),
        P("row", "rep"),
    )
    return jax.shard_map(
        on_device,
        mesh=mesh,
        in_specs=placed,
        out_specs=(P("row", "rep"), P(None, "rep"), P("rep")),
        check_vma=False,
    )
```

```python
import jax
import jax.numpy as jnp
from jax import lax
from jax.sharding import PartitionSpec as P


def sum_over(x, axis_name, count):
    rows = x.shape[0]
    pieces = x.reshape((count, rows // count) + x.shape[1:])
    got = lax.all_to_all(pieces, axis_name, 0, 0, tiled=True)
    reduced = jnp.sum(got.astype(jnp.float32), axis=0)
    return reduced


def spread(x, axis_name, count):
    wide = jnp.broadcast_to(x[None], (count,) + x.shape)
    return lax.all_to_all(wide, axis_name, 0, 0, tiled=True)


def on_device(features, owner_index, block_cols, block_count, tiles, weight, bias, grad_out):
    rows_part, cols_dev = features.shape
    parts = lax.axis_size("row")
    reps = lax.axis_size("rep")
    per_pair = rows_part // parts
    rb, slots_dev, size_blk = tiles.shape[0], tiles.shape[1], tiles.shape[2]

    destination = owner_index // rows_part
    same = destination[:, None] == destination[None, :]
    before = jnp.arange(rows_part)[:, None] > jnp.arange(rows_part)[None, :]
    rank = jnp.sum(same & before, axis=1)
    slot = rank * parts + destination
    place = (slot[:, None] == jnp.arange(rows_part)[None, :]).astype(jnp.bfloat16)
    pos_row = (owner_index % rows_part).astype(jnp.bfloat16)
    loader = jnp.concatenate([features.T, pos_row[None, :]], axis=0)
    packet = jnp.dot(loader, place, preferred_element_type=jnp.float32).astype(jnp.bfloat16)
    width = cols_dev + 1
    packet = packet.reshape(width, per_pair, parts)
    wide = jnp.broadcast_to(packet[None], (parts,) + packet.shape)
    grouped = lax.all_to_all(wide, "row", 0, 2, tiled=True)[0]
    pos = grouped[cols_dev].T.astype(jnp.int32)
    values = grouped[:cols_dev]

    cols_all = lax.all_gather(block_cols, "rep", axis=1, tiled=True)
    part_of = cols_all // rb
    half_of = cols_all % rb
    part_ids = jnp.arange(parts, dtype=jnp.int32)
    hit = part_of[None, :, :] == part_ids[:, None, None]
    half = jnp.max(jnp.where(hit, half_of[None, :, :], 0), axis=(1, 2))
    node_ids = jnp.arange(size_blk, dtype=jnp.int32)
    target = half[:, None, None] * size_blk + node_ids[None, None, :]
    pick = (pos[:, :, None] == target).astype(jnp.bfloat16)
    needed = jnp.einsum("fgq,qgn->qfn", grouped, pick, preferred_element_type=jnp.float32).astype(jnp.bfloat16)
    needed = needed[:, :cols_dev, :]

    peer_parts = part_of.reshape(rb, reps, slots_dev).transpose(1, 0, 2).reshape(-1)
    choose = (peer_parts[:, None] == part_ids[None, :]).astype(jnp.bfloat16)
    outgoing = jnp.dot(choose, needed.reshape(parts, -1), preferred_element_type=jnp.float32)
    outgoing = outgoing.astype(jnp.bfloat16).reshape(reps, rb, slots_dev, cols_dev, size_blk)
    incoming = lax.all_to_all(outgoing, "rep", 0, 0, tiled=True)

    slot_ids = lax.axis_index("rep") * slots_dev + jnp.arange(slots_dev, dtype=jnp.int32)
    live = slot_ids[None, :] < block_count[:, None]
    tiles_live = jnp.where(live[:, :, None, None], tiles, jnp.zeros_like(tiles))
    partial = jnp.einsum("rsin,jrsfn->rijf", tiles_live, incoming, preferred_element_type=jnp.float32)
    partial = partial.reshape(rows_part, reps * cols_dev)

    shares = spread(partial.astype(jnp.bfloat16), "rep", reps)
    agg = jnp.sum(shares.astype(jnp.float32), axis=0).astype(jnp.bfloat16)

    pre = jnp.dot(agg, weight, preferred_element_type=jnp.float32) + bias
    hidden = jax.nn.silu(pre).astype(jnp.bfloat16)
    sig = jax.nn.sigmoid(pre)
    dpre = (grad_out.astype(jnp.float32) * sig * (1.0 + pre * (1.0 - sig))).astype(jnp.bfloat16)
    weight_term = jnp.dot(agg.T, dpre, preferred_element_type=jnp.float32)
    bias_term = jnp.sum(dpre.astype(jnp.float32), axis=0)

    n_in, n_out = weight_term.shape
    bias_row = jnp.pad(bias_term, (0, n_in - n_out))[None, :]
    stacked = jnp.concatenate([weight_term.T, bias_row], axis=0)
    per = -(-stacked.shape[0] // parts)
    stacked = jnp.pad(stacked, ((0, parts * per - stacked.shape[0]), (0, 0)))
    total = spread(sum_over(stacked, "row", parts), "row", parts).reshape(parts * per, n_in)
    weight_grad = total[:n_out].T
    bias_grad = total[n_out, :n_out]
    return (hidden, weight_grad, bias_grad)


def solution(mesh):
    placed = (
        P("row", "rep"),
        P("row"),
        P("row", "rep"),
        P("row"),
        P("row", "rep", None, None),
        P(None, "rep"),
        P("rep"),
        P("row", "rep"),
    )
    return jax.shard_map(
        on_device,
        mesh=mesh,
        in_specs=placed,
        out_specs=(P("row", "rep"), P(None, "rep"), P("rep")),
        check_vma=False,
    )
```
